128 devices in a mesh: rep: 4 (over z), node: 4 (over y), local: 8 (over x, core).
Axes of the slice: x: 4, y: 4, z: 4, core: 2. Of those that a mesh axis runs over, the one named last changes fastest.
Arguments:
- tokens: bfloat16 [8192, 7168], P(('rep', 'node', 'local')), parts along dimension 0, may hold values from -6 to 6
- expert_ids: int32 [8192, 8], P(('rep', 'node', 'local')), parts along dimension 0, may hold values from 0 to 127, as said below
- node_groups: int32 [8192, 2], P(('rep', 'node', 'local')), parts along dimension 0, may hold values from 0 to 3, as said below
- gate_levels: int32 [8192, 8], P(('rep', 'node', 'local')), parts along dimension 0, may hold values from 1 to 255
- expert_seeds: int32 [128], P(('node', 'local')), may hold values from 0 to 999999999
Outputs:
- routed_out: bfloat16 [8192, 7168], P(('rep', 'node', 'local')), parts along dimension 0
The draws below stay inside these ranges and needn't reach their ends.
There are 4 independent parts, one for each index of `rep`. The reference program is written for one: setup_inputs(seed, part) draws one part's arguments, and reference() takes and returns one part's arrays. A program takes and returns all parts, laid end to end along the dimension named above; an argument that names none is the same for every part. Nothing has to cross between parts.
Inputs may be any that keep to these rules, and one draw needn't show every extreme that they name: `expert_ids`: each row names 8 different experts; expert e belongs to node group e // 32. `node_groups`: each row names 2 different node groups.
All inputs are finite; a program needn't handle non-finite values.
Results may differ from the reference program's by a relative error of at most 0.0085.
Values may be sent and summed in bfloat16 or wider, within the bound.
No kernel may reach another device: no remote copies, remote signals or barrier semaphores. Data moves between devices by JAX's collectives and lax.ppermute only.
A program may use at most 192 MiB of HBM per device.

```python
import math
import jax
import jax.numpy as jnp
from jax import lax

D = 7168
FF = 1024
TOP = 8
GROUP_PICK = 2
TOK_DEV = 64
GROUPS = 4
GROUP_EXPERTS = 32
EXPERTS = 128
TOKENS = 2048
CAP = 4
N_NODE = 4
N_LOCAL = 8


def routing_draw(key):
    group_key = jax.random.fold_in(key, 101)
    hot_key = jax.random.fold_in(key, 202)
    score_key = jax.random.fold_in(key, 303)
    group_range = jnp.arange(GROUPS, dtype=jnp.int32)
    group_score = jax.random.randint(group_key, (TOKENS, GROUPS), 0, 1 << 20, dtype=jnp.int32) * GROUPS + group_range[None, :]
    unused_groups, chosen_groups = lax.top_k(group_score, GROUP_PICK)
    expert_range = jnp.arange(EXPERTS, dtype=jnp.int32)
    in_group = jnp.any((expert_range // GROUP_EXPERTS)[None, None, :] == chosen_groups[:, :, None], axis=1)
    hot_flag = jax.random.randint(hot_key, (EXPERTS,), 0, 6, dtype=jnp.int32) == 0
    base_score = jax.random.randint(score_key, (TOKENS, EXPERTS), 0, 1000, dtype=jnp.int32)
    expert_score = base_score + 150 * hot_flag.astype(jnp.int32)[None, :] + 600 * in_group.astype(jnp.int32)
    unused_values, chosen_experts = lax.top_k(expert_score * EXPERTS + expert_range[None, :], TOP)
    return (chosen_groups.astype(jnp.int32), chosen_experts.astype(jnp.int32))


def draw_node_groups(key, part):
    return routing_draw(key)[0]


def draw_expert_ids(key, part):
    return routing_draw(key)[1]


def with_ends(values, own_key, smallest, largest):
    index_at = [jax.random.randint(jax.random.fold_in(own_key, axis), (), 0, length) for axis, length in enumerate(values.shape)]
    longest = values.shape.index(max(values.shape))
    neighbour = index_at[:longest] + [(index_at[longest] + 1) % values.shape[longest]] + index_at[longest + 1:]
    return values.at[tuple(index_at)].set(smallest).at[tuple(neighbour)].set(largest)


def block_levels(rng, shape, shards, smallest, largest):
    def one(dim, blocks):
        draws = jax.random.uniform(jax.random.fold_in(jax.random.fold_in(rng, 6), dim), (blocks,), jnp.float32, smallest / len(shards), largest / len(shards))
        return jnp.repeat(jnp.exp(draws), shape[dim] // blocks).reshape((-1,) + (1,) * (len(shape) - dim - 1))

    factor_of = one(*shards[0])
    for cut in shards[1:]:
        factor_of = factor_of * one(*cut)
    return factor_of


def gaussian(rng, dims, spread, most, shards=(), held_as=jnp.bfloat16):
    factor_of = block_levels(rng, dims, shards, -0.22, 0.18) if shards else 1.0
    array = jax.random.normal(rng, dims, jnp.float32) * spread * factor_of
    return jnp.minimum(jnp.maximum(array, -most), most).astype(held_as)


def setup_inputs(seed: int = 0, part: int = 0) -> dict:
    keys = jax.random.split(jax.random.key(seed), 6)
    part_splits = jax.random.split(jax.random.fold_in(keys[5], part), 6)
    return {
        "tokens": gaussian(part_splits[0], (TOKENS, D), 1.0, 6.0, ((0, 32),)),
        "expert_ids": draw_expert_ids(jax.random.fold_in(jax.random.fold_in(keys[5], part), 71), part),
        "node_groups": draw_node_groups(jax.random.fold_in(jax.random.fold_in(keys[5], part), 71), part),
        "gate_levels": with_ends(jax.random.randint(part_splits[3], (TOKENS, TOP), 1, 256), jax.random.fold_in(part_splits[3], 1), 1, 255).astype(jnp.int32),
        "expert_seeds": with_ends(jax.random.randint(keys[4], (EXPERTS,), 0, 1000000000), jax.random.fold_in(keys[4], 1), 0, 999999999).astype(jnp.int32),
    }


route_scale = 2.5
salt_gate = 1013904223
salt_up = 1664525
salt_down = 22695477

def hashed_weight(expert_seed, salt_value, row_count, column_count, fan_in):
    row_index = lax.broadcasted_iota(jnp.int32, (row_count, column_count), 0)
    column_index = lax.broadcasted_iota(jnp.int32, (row_count, column_count), 1)
    hashed = (row_index * column_count + column_index) * 747796405 + expert_seed * 1103515245 + salt_value
    hashed = hashed ^ hashed >> 15
    hashed = hashed * 277803737
    hashed = hashed ^ hashed >> 13
    hashed = hashed * 668265263
    hashed = hashed ^ hashed >> 16
    sixteen_bits = (hashed >> 8 & 65535).astype(jnp.float32)
    return ((sixteen_bits - 32767.5) * (math.sqrt(3.0 / fan_in) / 32768.0)).astype(jnp.bfloat16)

def expert_block(block_rows, expert_seed):
    weight_gate = hashed_weight(expert_seed, salt_gate, D, FF, D)
    weight_up = hashed_weight(expert_seed, salt_up, D, FF, D)
    weight_down = hashed_weight(expert_seed, salt_down, FF, D, FF)
    gate_part = jnp.dot(block_rows, weight_gate, preferred_element_type=jnp.float32)
    up_part = jnp.dot(block_rows, weight_up, preferred_element_type=jnp.float32)
    hidden = (jax.nn.silu(gate_part) * up_part).astype(jnp.bfloat16)
    return jnp.dot(hidden, weight_down, preferred_element_type=jnp.float32).astype(jnp.bfloat16)

def group_mask(expert_ids, node_groups, group_size):
    return jnp.any((expert_ids // group_size)[:, :, None] == node_groups[:, None, :], axis=2)

def gate_of(gate_levels, in_group):
    levels = gate_levels.astype(jnp.float32)
    return route_scale * levels * in_group.astype(jnp.float32) / lax.optimization_barrier(jnp.sum(levels, axis=1, keepdims=True))

def rank_of(expert_ids, in_group, blocks, capacity, experts_total):
    expert_range = jnp.arange(experts_total, dtype=jnp.int32)
    hit_table = ((expert_ids[:, :, None] == expert_range[None, None, :]) & in_group[:, :, None]).astype(jnp.int32)
    present = lax.optimization_barrier(jnp.sum(hit_table, axis=1, dtype=jnp.int32))
    blocked = present.reshape(blocks, -1, experts_total)
    before = (jnp.cumsum(blocked, axis=1, dtype=jnp.int32) - blocked).reshape(-1, experts_total)
    slot_rank = lax.optimization_barrier(jnp.sum(hit_table * before[:, None, :], axis=2, dtype=jnp.int32)).astype(jnp.int32)
    kept_mask = in_group & (slot_rank < capacity)
    return (slot_rank, kept_mask)

def reference(tokens, expert_ids, node_groups, gate_levels, expert_seeds):
    sources = N_NODE * N_LOCAL
    in_group = group_mask(expert_ids, node_groups, GROUP_EXPERTS)
    gate_share = gate_of(gate_levels, in_group)
    slot_rank, kept_mask = rank_of(expert_ids, in_group, sources, CAP, EXPERTS)
    token_index = lax.broadcasted_iota(jnp.int32, (TOKENS, TOP), 0)
    source_index = token_index // TOK_DEV
    slot_total = EXPERTS * sources * CAP
    slot_index = jnp.where(kept_mask, (expert_ids * sources + source_index) * CAP + slot_rank, slot_total).astype(jnp.int32)
    slot_token = jnp.full((slot_total,), TOKENS, jnp.int32).at[slot_index.reshape(-1)].set(token_index.reshape(-1), mode='drop')
    slot_gate = jnp.zeros((slot_total,), jnp.float32).at[slot_index.reshape(-1)].set(gate_share.reshape(-1), mode='drop')
    padded = jnp.concatenate([tokens, jnp.zeros((1, D), tokens.dtype)], axis=0)

    def per_expert(running, scan_item):
        expert_seed, token_list, gate_list = scan_item
        outputs = expert_block(padded[token_list], expert_seed)
        running = running.at[token_list].add(gate_list[:, None] * outputs.astype(jnp.float32), mode='drop')
        return (running, None)
    summed, unused = lax.scan(per_expert, jnp.zeros((TOKENS, D), jnp.float32), (expert_seeds, slot_token.reshape(EXPERTS, -1), slot_gate.reshape(EXPERTS, -1)))
    return summed.astype(jnp.bfloat16)
```

```python
import math

import jax
import jax.numpy as jnp
from jax import lax
from jax.sharding import PartitionSpec as P

D = 7168
FF = 1024
TOP = 8
EXP_DEV = 4


route_scale = 2.5
salt_gate = 1013904223
salt_up = 1664525
salt_down = 22695477


def hashed_weight(expert_seed, salt_value, row_count, column_count, fan_in):
    row_index = lax.broadcasted_iota(jnp.int32, (row_count, column_count), 0)
    column_index = lax.broadcasted_iota(jnp.int32, (row_count, column_count), 1)
    hashed = (
        (row_index * column_count + column_index) * 747796405
        + expert_seed * 1103515245
        + salt_value
    )
    hashed = hashed ^ hashed >> 15
    hashed = hashed * 277803737
    hashed = hashed ^ hashed >> 13
    hashed = hashed * 668265263
    hashed = hashed ^ hashed >> 16
    sixteen_bits = (hashed >> 8 & 65535).astype(jnp.float32)
    return ((sixteen_bits - 32767.5) * (math.sqrt(3.0 / fan_in) / 32768.0)).astype(jnp.bfloat16)


def expert_block(block_rows, expert_seed):
    weight_gate = hashed_weight(expert_seed, salt_gate, D, FF, D)
    weight_up = hashed_weight(expert_seed, salt_up, D, FF, D)
    weight_down = hashed_weight(expert_seed, salt_down, FF, D, FF)
    gate_part = jnp.dot(block_rows, weight_gate, preferred_element_type=jnp.float32)
    up_part = jnp.dot(block_rows, weight_up, preferred_element_type=jnp.float32)
    hidden = (jax.nn.silu(gate_part) * up_part).astype(jnp.bfloat16)
    return jnp.dot(hidden, weight_down, preferred_element_type=jnp.float32).astype(jnp.bfloat16)


def run_experts(expert_rows, local_seeds):

    def per_expert(running, scan_item):
        expert_seed, block_rows = scan_item
        return (running, expert_block(block_rows, expert_seed))

    unused, outputs = lax.scan(per_expert, jnp.zeros((), jnp.int32), (local_seeds, expert_rows))
    return outputs


def group_mask(expert_ids, node_groups, group_size):
    return jnp.any((expert_ids // group_size)[:, :, None] == node_groups[:, None, :], axis=2)


def gate_of(gate_levels, in_group):
    levels = gate_levels.astype(jnp.float32)
    return (
        route_scale * levels * in_group.astype(jnp.float32) / jnp.sum(levels, axis=1, keepdims=True)
    )


def rank_of(expert_ids, in_group, blocks, capacity, experts_total):
    expert_range = jnp.arange(experts_total, dtype=jnp.int32)
    hit_table = (
        (expert_ids[:, :, None] == expert_range[None, None, :]) & in_group[:, :, None]
    ).astype(jnp.int32)
    present = jnp.sum(hit_table, axis=1, dtype=jnp.int32)
    blocked = present.reshape(blocks, -1, experts_total)
    before = (jnp.cumsum(blocked, axis=1, dtype=jnp.int32) - blocked).reshape(-1, experts_total)
    slot_rank = jnp.sum(hit_table * before[:, None, :], axis=2, dtype=jnp.int32)
    kept_mask = in_group & (slot_rank < capacity)
    return (slot_rank, kept_mask)


def fill_slots(row_block, slot_index, slot_total):
    row_count = row_block.shape[0]
    token_index = lax.broadcasted_iota(jnp.int32, slot_index.shape, 0)
    slot_token = (
        jnp.full((slot_total,), row_count, jnp.int32)
        .at[slot_index.reshape(-1)]
        .set(token_index.reshape(-1), mode="drop")
    )
    padded = jnp.concatenate(
        [row_block, jnp.zeros((1, row_block.shape[1]), row_block.dtype)], axis=0
    )
    return padded[slot_token]


def combine_rows(returned, slot_index, gate_share):
    padded = jnp.concatenate([returned, jnp.zeros((1, returned.shape[1]), returned.dtype)], axis=0)
    picked = padded[slot_index]
    return jnp.einsum("tj,tjd->td", gate_share, picked.astype(jnp.float32))


def on_device(tokens, expert_ids, node_groups, gate_levels, expert_seeds):
    tok_count = tokens.shape[0]
    width = tokens.shape[1]
    axes = ("rep", "node", "local")
    rep_count = lax.axis_size("rep")
    plane_count = lax.axis_size(("node", "local"))
    local_count = lax.axis_size("local")
    seeds_here = expert_seeds.shape[0]
    assert seeds_here == rep_count
    experts_total = seeds_here * plane_count
    capacity = max(2, tok_count * TOP // experts_total)
    group_size = seeds_here * local_count
    in_group = group_mask(expert_ids, node_groups, group_size)
    gate_share = gate_of(gate_levels, in_group)
    slot_rank, kept_mask = rank_of(expert_ids, in_group, 1, capacity, experts_total)
    dest = (expert_ids % seeds_here) * plane_count + expert_ids // seeds_here
    slot_total = experts_total * capacity
    slot_index = jnp.where(kept_mask, dest * capacity + slot_rank, slot_total)
    send_rows = fill_slots(tokens, slot_index, slot_total)
    arrived = lax.all_to_all(send_rows, axes, split_axis=0, concat_axis=0, tiled=True)
    my_seed = expert_seeds[lax.axis_index("rep")]
    results = expert_block(arrived, my_seed)
    returned = lax.all_to_all(results, axes, split_axis=0, concat_axis=0, tiled=True)
    return combine_rows(returned, slot_index, gate_share).astype(jnp.bfloat16)


def solution(mesh):
    in_specs = (
        P(("rep", "node", "local"), None),
        P(("rep", "node", "local"), None),
        P(("rep", "node", "local"), None),
        P(("rep", "node", "local"), None),
        P(("node", "local")),
    )
    out_specs = P(("rep", "node", "local"), None)
    return jax.shard_map(
        on_device, mesh=mesh, in_specs=in_specs, out_specs=out_specs, check_vma=False
    )
```

```python
import math

import jax
import jax.numpy as jnp
from jax import lax
from jax.sharding import PartitionSpec as P

D = 7168
FF = 1024
TOP = 8
EXP_DEV = 4


route_scale = 2.5
salt_gate = 1013904223
salt_up = 1664525
salt_down = 22695477


def hashed_weight(expert_seed, salt_value, row_count, column_count, fan_in):
    row_index = lax.broadcasted_iota(jnp.int32, (row_count, column_count), 0)
    column_index = lax.broadcasted_iota(jnp.int32, (row_count, column_count), 1)
    hashed = (
        (row_index * column_count + column_index) * 747796405
        + expert_seed * 1103515245
        + salt_value
    )
    hashed = hashed ^ hashed >> 15
    hashed = hashed * 277803737
    hashed = hashed ^ hashed >> 13
    hashed = hashed * 668265263
    hashed = hashed ^ hashed >> 16
    sixteen_bits = (hashed >> 8 & 65535).astype(jnp.float32)
    return ((sixteen_bits - 32767.5) * (math.sqrt(3.0 / fan_in) / 32768.0)).astype(jnp.bfloat16)


def expert_block(block_rows, expert_seed):
    weight_gate = hashed_weight(expert_seed, salt_gate, D, FF, D)
    weight_up = hashed_weight(expert_seed, salt_up, D, FF, D)
    weight_down = hashed_weight(expert_seed, salt_down, FF, D, FF)
    gate_part = jnp.dot(block_rows, weight_gate, preferred_element_type=jnp.float32)
    up_part = jnp.dot(block_rows, weight_up, preferred_element_type=jnp.float32)
    hidden = (jax.nn.silu(gate_part) * up_part).astype(jnp.bfloat16)
    return jnp.dot(hidden, weight_down, preferred_element_type=jnp.float32).astype(jnp.bfloat16)


def run_experts(expert_rows, local_seeds):

    def per_expert(running, scan_item):
        expert_seed, block_rows = scan_item
        return (running, expert_block(block_rows, expert_seed))

    unused, outputs = lax.scan(per_expert, jnp.zeros((), jnp.int32), (local_seeds, expert_rows))
    return outputs


def group_mask(expert_ids, node_groups, group_size):
    return jnp.any((expert_ids // group_size)[:, :, None] == node_groups[:, None, :], axis=2)


def gate_of(gate_levels, in_group):
    levels = gate_levels.astype(jnp.float32)
    return (
        route_scale * levels * in_group.astype(jnp.float32) / jnp.sum(levels, axis=1, keepdims=True)
    )


def rank_of(expert_ids, in_group, blocks, capacity, experts_total):
    expert_range = jnp.arange(experts_total, dtype=jnp.int32)
    hit_table = (
        (expert_ids[:, :, None] == expert_range[None, None, :]) & in_group[:, :, None]
    ).astype(jnp.int32)
    present = jnp.sum(hit_table, axis=1, dtype=jnp.int32)
    blocked = present.reshape(blocks, -1, experts_total)
    before = (jnp.cumsum(blocked, axis=1, dtype=jnp.int32) - blocked).reshape(-1, experts_total)
    slot_rank = jnp.sum(hit_table * before[:, None, :], axis=2, dtype=jnp.int32)
    kept_mask = in_group & (slot_rank < capacity)
    return (slot_rank, kept_mask)


def fill_slots(row_block, slot_index, slot_total):
    row_count = row_block.shape[0]
    token_index = lax.broadcasted_iota(jnp.int32, slot_index.shape, 0)
    slot_token = (
        jnp.full((slot_total,), row_count, jnp.int32)
        .at[slot_index.reshape(-1)]
        .set(token_index.reshape(-1), mode="drop")
    )
    padded = jnp.concatenate(
        [row_block, jnp.zeros((1, row_block.shape[1]), row_block.dtype)], axis=0
    )
    return padded[slot_token]


def combine_rows(returned, slot_index, gate_share):
    padded = jnp.concatenate([returned, jnp.zeros((1, returned.shape[1]), returned.dtype)], axis=0)
    picked = padded[slot_index]
    return jnp.einsum("tj,tjd->td", gate_share, picked.astype(jnp.float32))


def expert_weights(expert_seed):
    weight_gate = hashed_weight(expert_seed, salt_gate, D, FF, D)
    weight_up = hashed_weight(expert_seed, salt_up, D, FF, D)
    weight_down = hashed_weight(expert_seed, salt_down, FF, D, FF)
    return lax.optimization_barrier((weight_gate, weight_up, weight_down))


def expert_rows(block_rows, weights):
    weight_gate, weight_up, weight_down = weights
    gate_part = jnp.einsum("sct,tf->scf", block_rows, weight_gate, preferred_element_type=jnp.float32)
    up_part = jnp.einsum("sct,tf->scf", block_rows, weight_up, preferred_element_type=jnp.float32)
    hidden = (jax.nn.silu(gate_part) * up_part).astype(jnp.bfloat16)
    return jnp.einsum("scf,ft->sct", hidden, weight_down, preferred_element_type=jnp.float32).astype(
        jnp.bfloat16
    )


def on_device(tokens, expert_ids, node_groups, gate_levels, expert_seeds):
    tok_count = tokens.shape[0]
    width = tokens.shape[1]
    axes = ("rep", "node", "local")
    rep_count = lax.axis_size("rep")
    plane_count = lax.axis_size(("node", "local"))
    local_count = lax.axis_size("local")
    seeds_here = expert_seeds.shape[0]
    assert seeds_here == rep_count
    experts_total = seeds_here * plane_count
    devices_all = experts_total
    capacity = max(2, tok_count * TOP // experts_total)
    group_size = seeds_here * local_count
    in_group = group_mask(expert_ids, node_groups, group_size)
    gate_share = gate_of(gate_levels, in_group)
    slot_rank, kept_mask = rank_of(expert_ids, in_group, 1, capacity, experts_total)
    dest = (expert_ids % seeds_here) * plane_count + expert_ids // seeds_here
    slot_total = experts_total * capacity
    slot_index = jnp.where(kept_mask, dest * capacity + slot_rank, slot_total)
    token_index = lax.broadcasted_iota(jnp.int32, slot_index.shape, 0)
    slot_token = (
        jnp.full((slot_total,), tok_count, jnp.int32)
        .at[slot_index.reshape(-1)]
        .set(token_index.reshape(-1), mode="drop")
    )
    padded = jnp.concatenate([tokens, jnp.zeros((1, width), tokens.dtype)], axis=0)
    send_rows = padded[slot_token.reshape(devices_all, capacity)]
    weights = expert_weights(expert_seeds[lax.axis_index("rep")])
    arrived = lax.all_to_all(send_rows, axes, split_axis=0, concat_axis=0, tiled=True)
    results = expert_rows(arrived, weights)
    returned = lax.all_to_all(results, axes, split_axis=0, concat_axis=0, tiled=True)
    safe_dest = jnp.where(kept_mask, dest, 0)
    safe_rank = jnp.where(kept_mask, slot_rank, 0)
    picked = returned[safe_dest, safe_rank]
    share = jnp.where(kept_mask, gate_share, 0.0)
    return jnp.einsum("tj,tjd->td", share, picked.astype(jnp.float32)).astype(jnp.bfloat16)


def solution(mesh):
    in_specs = (
        P(("rep", "node", "local"), None),
        P(("rep", "node", "local"), None),
        P(("rep", "node", "local"), None),
        P(("rep", "node", "local"), None),
        P(("node", "local")),
    )
    out_specs = P(("rep", "node", "local"), None)
    return jax.shard_map(
        on_device, mesh=mesh, in_specs=in_specs, out_specs=out_specs, check_vma=False
    )
```

```python
import math

import jax
import jax.numpy as jnp
from jax import lax
from jax.sharding import PartitionSpec as P

D = 7168
FF = 1024
TOP = 8
EXP_DEV = 4


route_scale = 2.5
salt_gate = 1013904223
salt_up = 1664525
salt_down = 22695477


def hashed_weight(expert_seed, salt_value, row_count, column_count, fan_in):
    row_index = lax.broadcasted_iota(jnp.int32, (row_count, column_count), 0)
    column_index = lax.broadcasted_iota(jnp.int32, (row_count, column_count), 1)
    hashed = (
        (row_index * column_count + column_index) * 747796405
        + expert_seed * 1103515245
        + salt_value
    )
    hashed = hashed ^ hashed >> 15
    hashed = hashed * 277803737
    hashed = hashed ^ hashed >> 13
    hashed = hashed * 668265263
    hashed = hashed ^ hashed >> 16
    sixteen_bits = (hashed >> 8 & 65535).astype(jnp.float32)
    return ((sixteen_bits - 32767.5) * (math.sqrt(3.0 / fan_in) / 32768.0)).astype(jnp.bfloat16)


def expert_block(block_rows, expert_seed):
    weight_gate = hashed_weight(expert_seed, salt_gate, D, FF, D)
    weight_up = hashed_weight(expert_seed, salt_up, D, FF, D)
    weight_down = hashed_weight(expert_seed, salt_down, FF, D, FF)
    gate_part = jnp.dot(block_rows, weight_gate, preferred_element_type=jnp.float32)
    up_part = jnp.dot(block_rows, weight_up, preferred_element_type=jnp.float32)
    hidden = (jax.nn.silu(gate_part) * up_part).astype(jnp.bfloat16)
    return jnp.dot(hidden, weight_down, preferred_element_type=jnp.float32).astype(jnp.bfloat16)


def run_experts(expert_rows, local_seeds):

    def per_expert(running, scan_item):
        expert_seed, block_rows = scan_item
        return (running, expert_block(block_rows, expert_seed))

    unused, outputs = lax.scan(per_expert, jnp.zeros((), jnp.int32), (local_seeds, expert_rows))
    return outputs


def group_mask(expert_ids, node_groups, group_size):
    return jnp.any((expert_ids // group_size)[:, :, None] == node_groups[:, None, :], axis=2)


def gate_of(gate_levels, in_group):
    levels = gate_levels.astype(jnp.float32)
    return (
        route_scale * levels * in_group.astype(jnp.float32) / jnp.sum(levels, axis=1, keepdims=True)
    )


def rank_of(expert_ids, in_group, blocks, capacity, experts_total):
    expert_range = jnp.arange(experts_total, dtype=jnp.int32)
    hit_table = (
        (expert_ids[:, :, None] == expert_range[None, None, :]) & in_group[:, :, None]
    ).astype(jnp.int32)
    present = jnp.sum(hit_table, axis=1, dtype=jnp.int32)
    blocked = present.reshape(blocks, -1, experts_total)
    before = (jnp.cumsum(blocked, axis=1, dtype=jnp.int32) - blocked).reshape(-1, experts_total)
    slot_rank = jnp.sum(hit_table * before[:, None, :], axis=2, dtype=jnp.int32)
    kept_mask = in_group & (slot_rank < capacity)
    return (slot_rank, kept_mask)


def fill_slots(row_block, slot_index, slot_total):
    row_count = row_block.shape[0]
    token_index = lax.broadcasted_iota(jnp.int32, slot_index.shape, 0)
    slot_token = (
        jnp.full((slot_total,), row_count, jnp.int32)
        .at[slot_index.reshape(-1)]
        .set(token_index.reshape(-1), mode="drop")
    )
    padded = jnp.concatenate(
        [row_block, jnp.zeros((1, row_block.shape[1]), row_block.dtype)], axis=0
    )
    return padded[slot_token]


def combine_rows(returned, slot_index, gate_share):
    padded = jnp.concatenate([returned, jnp.zeros((1, returned.shape[1]), returned.dtype)], axis=0)
    picked = padded[slot_index]
    return jnp.einsum("tj,tjd->td", gate_share, picked.astype(jnp.float32))


def expert_weights(expert_seed):
    weight_gate = hashed_weight(expert_seed, salt_gate, D, FF, D)
    weight_up = hashed_weight(expert_seed, salt_up, D, FF, D)
    weight_down = hashed_weight(expert_seed, salt_down, FF, D, FF)
    return lax.optimization_barrier((weight_gate, weight_up, weight_down))


def expert_rows(block_rows, weights):
    weight_gate, weight_up, weight_down = weights
    gate_part = jnp.einsum("sct,tf->scf", block_rows, weight_gate, preferred_element_type=jnp.float32)
    up_part = jnp.einsum("sct,tf->scf", block_rows, weight_up, preferred_element_type=jnp.float32)
    hidden = (jax.nn.silu(gate_part) * up_part).astype(jnp.bfloat16)
    return jnp.einsum("scf,ft->sct", hidden, weight_down, preferred_element_type=jnp.float32).astype(
        jnp.bfloat16
    )


def on_device(tokens, expert_ids, node_groups, gate_levels, expert_seeds):
    tok_count = tokens.shape[0]
    width = tokens.shape[1]
    axes = ("rep", "node", "local")
    rep_count = lax.axis_size("rep")
    plane_count = lax.axis_size(("node", "local"))
    local_count = lax.axis_size("local")
    seeds_here = expert_seeds.shape[0]
    assert seeds_here == rep_count
    experts_total = seeds_here * plane_count
    devices_all = experts_total
    capacity = max(2, tok_count * TOP // experts_total)
    group_size = seeds_here * local_count
    in_group = group_mask(expert_ids, node_groups, group_size)
    gate_share = gate_of(gate_levels, in_group)
    slot_rank, kept_mask = rank_of(expert_ids, in_group, 1, capacity, experts_total)
    dest = (expert_ids % seeds_here) * plane_count + expert_ids // seeds_here
    slot_total = experts_total * capacity
    slot_index = jnp.where(kept_mask, dest * capacity + slot_rank, slot_total)
    slot_range = jnp.arange(slot_total, dtype=jnp.int32)
    hit = slot_index[:, :, None] == slot_range[None, None, :]
    pick = jnp.any(hit, axis=1).astype(tokens.dtype)
    send_rows = jnp.einsum(
        "tsc,td->scd", pick.reshape(tok_count, devices_all, capacity), tokens,
        preferred_element_type=jnp.float32,
    ).astype(tokens.dtype)
    weights = expert_weights(expert_seeds[lax.axis_index("rep")])
    arrived = lax.all_to_all(send_rows, axes, split_axis=0, concat_axis=0, tiled=True)
    results = expert_rows(arrived, weights)
    returned = lax.all_to_all(results, axes, split_axis=0, concat_axis=0, tiled=True)
    share = jnp.where(kept_mask, gate_share, 0.0)
    combine = jnp.sum(jnp.where(hit, share[:, :, None], 0.0), axis=1)
    out = jnp.einsum(
        "tsc,scd->td", combine.reshape(tok_count, devices_all, capacity), returned,
        preferred_element_type=jnp.float32, precision=lax.Precision.HIGHEST,
    )
    return out.astype(jnp.bfloat16)


def solution(mesh):
    in_specs = (
        P(("rep", "node", "local"), None),
        P(("rep", "node", "local"), None),
        P(("rep", "node", "local"), None),
        P(("rep", "node", "local"), None),
        P(("node", "local")),
    )
    out_specs = P(("rep", "node", "local"), None)
    return jax.shard_map(
        on_device, mesh=mesh, in_specs=in_specs, out_specs=out_specs, check_vma=False
    )
```

```python
import math

import jax
import jax.numpy as jnp
from jax import lax
from jax.sharding import PartitionSpec as P

D = 7168
FF = 1024
TOP = 8
EXP_DEV = 4
CHUNKS = 2


route_scale = 2.5
salt_gate = 1013904223
salt_up = 1664525
salt_down = 22695477


def hashed_weight(expert_seed, salt_value, row_count, column_count, fan_in):
    row_index = lax.broadcasted_iota(jnp.int32, (row_count, column_count), 0)
    column_index = lax.broadcasted_iota(jnp.int32, (row_count, column_count), 1)
    hashed = (
        (row_index * column_count + column_index) * 747796405
        + expert_seed * 1103515245
        + salt_value
    )
    hashed = hashed ^ hashed >> 15
    hashed = hashed * 277803737
    hashed = hashed ^ hashed >> 13
    hashed = hashed * 668265263
    hashed = hashed ^ hashed >> 16
    sixteen_bits = (hashed >> 8 & 65535).astype(jnp.float32)
    return ((sixteen_bits - 32767.5) * (math.sqrt(3.0 / fan_in) / 32768.0)).astype(jnp.bfloat16)


def expert_block(block_rows, expert_seed):
    weight_gate = hashed_weight(expert_seed, salt_gate, D, FF, D)
    weight_up = hashed_weight(expert_seed, salt_up, D, FF, D)
    weight_down = hashed_weight(expert_seed, salt_down, FF, D, FF)
    gate_part = jnp.dot(block_rows, weight_gate, preferred_element_type=jnp.float32)
    up_part = jnp.dot(block_rows, weight_up, preferred_element_type=jnp.float32)
    hidden = (jax.nn.silu(gate_part) * up_part).astype(jnp.bfloat16)
    return jnp.dot(hidden, weight_down, preferred_element_type=jnp.float32).astype(jnp.bfloat16)


def run_experts(expert_rows, local_seeds):

    def per_expert(running, scan_item):
        expert_seed, block_rows = scan_item
        return (running, expert_block(block_rows, expert_seed))

    unused, outputs = lax.scan(per_expert, jnp.zeros((), jnp.int32), (local_seeds, expert_rows))
    return outputs


def group_mask(expert_ids, node_groups, group_size):
    return jnp.any((expert_ids // group_size)[:, :, None] == node_groups[:, None, :], axis=2)


def gate_of(gate_levels, in_group):
    levels = gate_levels.astype(jnp.float32)
    return (
        route_scale * levels * in_group.astype(jnp.float32) / jnp.sum(levels, axis=1, keepdims=True)
    )


def rank_of(expert_ids, in_group, blocks, capacity, experts_total):
    expert_range = jnp.arange(experts_total, dtype=jnp.int32)
    hit_table = (
        (expert_ids[:, :, None] == expert_range[None, None, :]) & in_group[:, :, None]
    ).astype(jnp.int32)
    present = jnp.sum(hit_table, axis=1, dtype=jnp.int32)
    blocked = present.reshape(blocks, -1, experts_total)
    before = (jnp.cumsum(blocked, axis=1, dtype=jnp.int32) - blocked).reshape(-1, experts_total)
    slot_rank = jnp.sum(hit_table * before[:, None, :], axis=2, dtype=jnp.int32)
    kept_mask = in_group & (slot_rank < capacity)
    return (slot_rank, kept_mask)


def fill_slots(row_block, slot_index, slot_total):
    row_count = row_block.shape[0]
    token_index = lax.broadcasted_iota(jnp.int32, slot_index.shape, 0)
    slot_token = (
        jnp.full((slot_total,), row_count, jnp.int32)
        .at[slot_index.reshape(-1)]
        .set(token_index.reshape(-1), mode="drop")
    )
    padded = jnp.concatenate(
        [row_block, jnp.zeros((1, row_block.shape[1]), row_block.dtype)], axis=0
    )
    return padded[slot_token]


def combine_rows(returned, slot_index, gate_share):
    padded = jnp.concatenate([returned, jnp.zeros((1, returned.shape[1]), returned.dtype)], axis=0)
    picked = padded[slot_index]
    return jnp.einsum("tj,tjd->td", gate_share, picked.astype(jnp.float32))


def expert_weights(expert_seed):
    weight_gate = hashed_weight(expert_seed, salt_gate, D, FF, D)
    weight_up = hashed_weight(expert_seed, salt_up, D, FF, D)
    weight_down = hashed_weight(expert_seed, salt_down, FF, D, FF)
    return lax.optimization_barrier((weight_gate, weight_up, weight_down))


def expert_rows(block_rows, weights):
    weight_gate, weight_up, weight_down = weights
    gate_part = jnp.einsum("sct,tf->scf", block_rows, weight_gate, preferred_element_type=jnp.float32)
    up_part = jnp.einsum("sct,tf->scf", block_rows, weight_up, preferred_element_type=jnp.float32)
    hidden = (jax.nn.silu(gate_part) * up_part).astype(jnp.bfloat16)
    return jnp.einsum("scf,ft->sct", hidden, weight_down, preferred_element_type=jnp.float32).astype(
        jnp.bfloat16
    )


def on_device(tokens, expert_ids, node_groups, gate_levels, expert_seeds):
    tok_count = tokens.shape[0]
    width = tokens.shape[1]
    axes = ("rep", "node", "local")
    rep_count = lax.axis_size("rep")
    plane_count = lax.axis_size(("node", "local"))
    local_count = lax.axis_size("local")
    seeds_here = expert_seeds.shape[0]
    assert seeds_here == rep_count
    experts_total = seeds_here * plane_count
    devices_all = experts_total
    capacity = max(2, tok_count * TOP // experts_total)
    group_size = seeds_here * local_count
    in_group = group_mask(expert_ids, node_groups, group_size)
    gate_share = gate_of(gate_levels, in_group)
    slot_rank, kept_mask = rank_of(expert_ids, in_group, 1, capacity, experts_total)
    dest = (expert_ids % seeds_here) * plane_count + expert_ids // seeds_here
    slot_total = experts_total * capacity
    slot_index = jnp.where(kept_mask, dest * capacity + slot_rank, slot_total)
    slot_range = jnp.arange(slot_total, dtype=jnp.int32)
    hit = slot_index[:, :, None] == slot_range[None, None, :]
    pick = jnp.any(hit, axis=1).astype(tokens.dtype)
    weights = expert_weights(expert_seeds[lax.axis_index("rep")])
    share = jnp.where(kept_mask, gate_share, 0.0)
    combine = jnp.sum(jnp.where(hit, share[:, :, None], 0.0), axis=1)
    pick = pick.reshape(tok_count, devices_all, capacity)
    combine = combine.reshape(tok_count, devices_all, capacity)
    chunk = capacity // CHUNKS
    out = None
    for k in range(CHUNKS):
        part = slice(k * chunk, (k + 1) * chunk)
        send_rows = jnp.einsum(
            "tsc,td->scd", pick[:, :, part], tokens, preferred_element_type=jnp.float32
        ).astype(tokens.dtype)
        arrived = lax.all_to_all(send_rows, axes, split_axis=0, concat_axis=0, tiled=True)
        results = expert_rows(arrived, weights)
        returned = lax.all_to_all(results, axes, split_axis=0, concat_axis=0, tiled=True)
        term = jnp.einsum(
            "tsc,scd->td", combine[:, :, part], returned,
            preferred_element_type=jnp.float32, precision=lax.Precision.HIGHEST,
        )
        out = term if out is None else out + term
    return out.astype(jnp.bfloat16)


def solution(mesh):
    in_specs = (
        P(("rep", "node", "local"), None),
        P(("rep", "node", "local"), None),
        P(("rep", "node", "local"), None),
        P(("rep", "node", "local"), None),
        P(("node", "local")),
    )
    out_specs = P(("rep", "node", "local"), None)
    return jax.shard_map(
        on_device, mesh=mesh, in_specs=in_specs, out_specs=out_specs, check_vma=False
    )
```

```python
import math

import jax
import jax.numpy as jnp
from jax import lax
from jax.sharding import PartitionSpec as P

D = 7168
FF = 1024
TOP = 8
EXP_DEV = 4
CHUNKS = 2


route_scale = 2.5
salt_gate = 1013904223
salt_up = 1664525
salt_down = 22695477


def hashed_weight(expert_seed, salt_value, row_count, column_count, fan_in):
    row_index = lax.broadcasted_iota(jnp.int32, (row_count, column_count), 0)
    column_index = lax.broadcasted_iota(jnp.int32, (row_count, column_count), 1)
    hashed = (
        (row_index * column_count + column_index) * 747796405
        + expert_seed * 1103515245
        + salt_value
    )
    hashed = hashed ^ hashed >> 15
    hashed = hashed * 277803737
    hashed = hashed ^ hashed >> 13
    hashed = hashed * 668265263
    hashed = hashed ^ hashed >> 16
    sixteen_bits = (hashed >> 8 & 65535).astype(jnp.float32)
    return ((sixteen_bits - 32767.5) * (math.sqrt(3.0 / fan_in) / 32768.0)).astype(jnp.bfloat16)


def expert_block(block_rows, expert_seed):
    weight_gate = hashed_weight(expert_seed, salt_gate, D, FF, D)
    weight_up = hashed_weight(expert_seed, salt_up, D, FF, D)
    weight_down = hashed_weight(expert_seed, salt_down, FF, D, FF)
    gate_part = jnp.dot(block_rows, weight_gate, preferred_element_type=jnp.float32)
    up_part = jnp.dot(block_rows, weight_up, preferred_element_type=jnp.float32)
    hidden = (jax.nn.silu(gate_part) * up_part).astype(jnp.bfloat16)
    return jnp.dot(hidden, weight_down, preferred_element_type=jnp.float32).astype(jnp.bfloat16)


def run_experts(expert_rows, local_seeds):

    def per_expert(running, scan_item):
        expert_seed, block_rows = scan_item
        return (running, expert_block(block_rows, expert_seed))

    unused, outputs = lax.scan(per_expert, jnp.zeros((), jnp.int32), (local_seeds, expert_rows))
    return outputs


def group_mask(expert_ids, node_groups, group_size):
    return jnp.any((expert_ids // group_size)[:, :, None] == node_groups[:, None, :], axis=2)


def gate_of(gate_levels, in_group):
    levels = gate_levels.astype(jnp.float32)
    return (
        route_scale * levels * in_group.astype(jnp.float32) / jnp.sum(levels, axis=1, keepdims=True)
    )


def rank_of(expert_ids, in_group, blocks, capacity, experts_total):
    expert_range = jnp.arange(experts_total, dtype=jnp.int32)
    hit_table = (
        (expert_ids[:, :, None] == expert_range[None, None, :]) & in_group[:, :, None]
    ).astype(jnp.int32)
    present = jnp.sum(hit_table, axis=1, dtype=jnp.int32)
    blocked = present.reshape(blocks, -1, experts_total)
    before = (jnp.cumsum(blocked, axis=1, dtype=jnp.int32) - blocked).reshape(-1, experts_total)
    slot_rank = jnp.sum(hit_table * before[:, None, :], axis=2, dtype=jnp.int32)
    kept_mask = in_group & (slot_rank < capacity)
    return (slot_rank, kept_mask)


def fill_slots(row_block, slot_index, slot_total):
    row_count = row_block.shape[0]
    token_index = lax.broadcasted_iota(jnp.int32, slot_index.shape, 0)
    slot_token = (
        jnp.full((slot_total,), row_count, jnp.int32)
        .at[slot_index.reshape(-1)]
        .set(token_index.reshape(-1), mode="drop")
    )
    padded = jnp.concatenate(
        [row_block, jnp.zeros((1, row_block.shape[1]), row_block.dtype)], axis=0
    )
    return padded[slot_token]


def combine_rows(returned, slot_index, gate_share):
    padded = jnp.concatenate([returned, jnp.zeros((1, returned.shape[1]), returned.dtype)], axis=0)
    picked = padded[slot_index]
    return jnp.einsum("tj,tjd->td", gate_share, picked.astype(jnp.float32))


def expert_weights(expert_seed):
    weight_gate = hashed_weight(expert_seed, salt_gate, D, FF, D)
    weight_up = hashed_weight(expert_seed, salt_up, D, FF, D)
    return lax.optimization_barrier((weight_gate, weight_up))


def down_weight(expert_seed):
    return lax.optimization_barrier(hashed_weight(expert_seed, salt_down, FF, D, FF))


def expert_rows(block_rows, weights):
    weight_gate, weight_up, weight_down = weights
    gate_part = jnp.einsum("sct,tf->scf", block_rows, weight_gate, preferred_element_type=jnp.float32)
    up_part = jnp.einsum("sct,tf->scf", block_rows, weight_up, preferred_element_type=jnp.float32)
    hidden = (jax.nn.silu(gate_part) * up_part).astype(jnp.bfloat16)
    return jnp.einsum("scf,ft->sct", hidden, weight_down, preferred_element_type=jnp.float32).astype(
        jnp.bfloat16
    )


def on_device(tokens, expert_ids, node_groups, gate_levels, expert_seeds):
    tok_count = tokens.shape[0]
    width = tokens.shape[1]
    axes = ("rep", "node", "local")
    rep_count = lax.axis_size("rep")
    plane_count = lax.axis_size(("node", "local"))
    local_count = lax.axis_size("local")
    seeds_here = expert_seeds.shape[0]
    assert seeds_here == rep_count
    experts_total = seeds_here * plane_count
    devices_all = experts_total
    capacity = max(2, tok_count * TOP // experts_total)
    group_size = seeds_here * local_count
    in_group = group_mask(expert_ids, node_groups, group_size)
    gate_share = gate_of(gate_levels, in_group)
    slot_rank, kept_mask = rank_of(expert_ids, in_group, 1, capacity, experts_total)
    dest = (expert_ids % seeds_here) * plane_count + expert_ids // seeds_here
    slot_total = experts_total * capacity
    slot_index = jnp.where(kept_mask, dest * capacity + slot_rank, slot_total)
    slot_range = jnp.arange(slot_total, dtype=jnp.int32)
    hit = slot_index[:, :, None] == slot_range[None, None, :]
    pick = jnp.any(hit, axis=1).astype(tokens.dtype)
    my_seed = expert_seeds[lax.axis_index("rep")]
    weights = expert_weights(my_seed)
    share = jnp.where(kept_mask, gate_share, 0.0)
    combine = jnp.sum(jnp.where(hit, share[:, :, None], 0.0), axis=1)
    pick = pick.reshape(tok_count, devices_all, capacity)
    combine = combine.reshape(tok_count, devices_all, capacity)
    chunk = capacity // CHUNKS
    out = None
    for k in range(CHUNKS):
        part = slice(k * chunk, (k + 1) * chunk)
        send_rows = jnp.einsum(
            "tsc,td->scd", pick[:, :, part], tokens, preferred_element_type=jnp.float32
        ).astype(tokens.dtype)
        arrived = lax.all_to_all(send_rows, axes, split_axis=0, concat_axis=0, tiled=True)
        if k == 0:
            arrived, later_seed = lax.optimization_barrier((arrived, my_seed))
            weights = weights + (down_weight(later_seed),)
        results = expert_rows(arrived, weights)
        returned = lax.all_to_all(results, axes, split_axis=0, concat_axis=0, tiled=True)
        term = jnp.einsum(
            "tsc,scd->td", combine[:, :, part], returned,
            preferred_element_type=jnp.float32, precision=lax.Precision.HIGHEST,
        )
        out = term if out is None else out + term
    return out.astype(jnp.bfloat16)


def solution(mesh):
    in_specs = (
        P(("rep", "node", "local"), None),
        P(("rep", "node", "local"), None),
        P(("rep", "node", "local"), None),
        P(("rep", "node", "local"), None),
        P(("node", "local")),
    )
    out_specs = P(("rep", "node", "local"), None)
    return jax.shard_map(
        on_device, mesh=mesh, in_specs=in_specs, out_specs=out_specs, check_vma=False
    )
```

```python
import math

import numpy as np

import jax
import jax.numpy as jnp
from jax import lax
from jax.sharding import PartitionSpec as P

D = 7168
FF = 1024
TOP = 8
EXP_DEV = 4
CHUNKS = 2


route_scale = 2.5
salt_gate = 1013904223
salt_up = 1664525
salt_down = 22695477


def wrapped(value):
    return ((value + 2**31) % 2**32) - 2**31


def hashed_weight(expert_seed, salt_value, row_count, column_count, fan_in):
    row_index = lax.broadcasted_iota(jnp.int32, (row_count, 1), 0)
    column_index = lax.broadcasted_iota(jnp.int32, (1, column_count), 1)
    row_term = row_index * wrapped(column_count * 747796405) + (expert_seed * 1103515245 + salt_value)
    hashed = row_term + column_index * 747796405
    hashed = hashed ^ hashed >> 15
    hashed = hashed * 277803737
    hashed = hashed ^ hashed >> 13
    hashed = hashed * 668265263
    shifted_bits = ((hashed ^ hashed >> 16) & 0xFFFF00).astype(jnp.float32)
    scale = np.float32(math.sqrt(3.0 / fan_in) / 32768.0) / np.float32(256.0)
    return ((shifted_bits - np.float32(32767.5 * 256)) * scale).astype(jnp.bfloat16)


def expert_block(block_rows, expert_seed):
    weight_gate = hashed_weight(expert_seed, salt_gate, D, FF, D)
    weight_up = hashed_weight(expert_seed, salt_up, D, FF, D)
    weight_down = hashed_weight(expert_seed, salt_down, FF, D, FF)
    gate_part = jnp.dot(block_rows, weight_gate, preferred_element_type=jnp.float32)
    up_part = jnp.dot(block_rows, weight_up, preferred_element_type=jnp.float32)
    hidden = (jax.nn.silu(gate_part) * up_part).astype(jnp.bfloat16)
    return jnp.dot(hidden, weight_down, preferred_element_type=jnp.float32).astype(jnp.bfloat16)


def run_experts(expert_rows, local_seeds):

    def per_expert(running, scan_item):
        expert_seed, block_rows = scan_item
        return (running, expert_block(block_rows, expert_seed))

    unused, outputs = lax.scan(per_expert, jnp.zeros((), jnp.int32), (local_seeds, expert_rows))
    return outputs


def group_mask(expert_ids, node_groups, group_size):
    return jnp.any((expert_ids // group_size)[:, :, None] == node_groups[:, None, :], axis=2)


def gate_of(gate_levels, in_group):
    levels = gate_levels.astype(jnp.float32)
    return (
        route_scale * levels * in_group.astype(jnp.float32) / jnp.sum(levels, axis=1, keepdims=True)
    )


def rank_of(expert_ids, in_group, blocks, capacity, experts_total):
    expert_range = jnp.arange(experts_total, dtype=jnp.int32)
    hit_table = (
        (expert_ids[:, :, None] == expert_range[None, None, :]) & in_group[:, :, None]
    ).astype(jnp.int32)
    present = jnp.sum(hit_table, axis=1, dtype=jnp.int32)
    blocked = present.reshape(blocks, -1, experts_total)
    before = (jnp.cumsum(blocked, axis=1, dtype=jnp.int32) - blocked).reshape(-1, experts_total)
    slot_rank = jnp.sum(hit_table * before[:, None, :], axis=2, dtype=jnp.int32)
    kept_mask = in_group & (slot_rank < capacity)
    return (slot_rank, kept_mask)


def fill_slots(row_block, slot_index, slot_total):
    row_count = row_block.shape[0]
    token_index = lax.broadcasted_iota(jnp.int32, slot_index.shape, 0)
    slot_token = (
        jnp.full((slot_total,), row_count, jnp.int32)
        .at[slot_index.reshape(-1)]
        .set(token_index.reshape(-1), mode="drop")
    )
    padded = jnp.concatenate(
        [row_block, jnp.zeros((1, row_block.shape[1]), row_block.dtype)], axis=0
    )
    return padded[slot_token]


def combine_rows(returned, slot_index, gate_share):
    padded = jnp.concatenate([returned, jnp.zeros((1, returned.shape[1]), returned.dtype)], axis=0)
    picked = padded[slot_index]
    return jnp.einsum("tj,tjd->td", gate_share, picked.astype(jnp.float32))


def expert_weights(expert_seed):
    weight_gate = hashed_weight(expert_seed, salt_gate, D, FF, D)
    weight_up = hashed_weight(expert_seed, salt_up, D, FF, D)
    return lax.optimization_barrier((weight_gate, weight_up))


def down_weight(expert_seed):
    return lax.optimization_barrier(hashed_weight(expert_seed, salt_down, FF, D, FF))


def expert_rows(block_rows, weights):
    weight_gate, weight_up, weight_down = weights
    gate_part = jnp.einsum("sct,tf->scf", block_rows, weight_gate, preferred_element_type=jnp.float32)
    up_part = jnp.einsum("sct,tf->scf", block_rows, weight_up, preferred_element_type=jnp.float32)
    hidden = (jax.nn.silu(gate_part) * up_part).astype(jnp.bfloat16)
    return jnp.einsum("scf,ft->sct", hidden, weight_down, preferred_element_type=jnp.float32).astype(
        jnp.bfloat16
    )


def on_device(tokens, expert_ids, node_groups, gate_levels, expert_seeds):
    tok_count = tokens.shape[0]
    width = tokens.shape[1]
    axes = ("rep", "node", "local")
    rep_count = lax.axis_size("rep")
    plane_count = lax.axis_size(("node", "local"))
    local_count = lax.axis_size("local")
    seeds_here = expert_seeds.shape[0]
    assert seeds_here == rep_count
    experts_total = seeds_here * plane_count
    devices_all = experts_total
    capacity = max(2, tok_count * TOP // experts_total)
    group_size = seeds_here * local_count
    in_group = group_mask(expert_ids, node_groups, group_size)
    gate_share = gate_of(gate_levels, in_group)
    slot_rank, kept_mask = rank_of(expert_ids, in_group, 1, capacity, experts_total)
    dest = (expert_ids % seeds_here) * plane_count + expert_ids // seeds_here
    slot_total = experts_total * capacity
    slot_index = jnp.where(kept_mask, dest * capacity + slot_rank, slot_total)
    slot_range = jnp.arange(slot_total, dtype=jnp.int32)
    hit = slot_index[:, :, None] == slot_range[None, None, :]
    pick = jnp.any(hit, axis=1).astype(tokens.dtype)
    my_seed = expert_seeds[lax.axis_index("rep")]
    weights = expert_weights(my_seed)
    share = jnp.where(kept_mask, gate_share, 0.0)
    combine = jnp.sum(jnp.where(hit, share[:, :, None], 0.0), axis=1)
    pick = pick.reshape(tok_count, devices_all, capacity)
    combine = combine.reshape(tok_count, devices_all, capacity)
    chunk = capacity // CHUNKS
    out = None
    for k in range(CHUNKS):
        part = slice(k * chunk, (k + 1) * chunk)
        send_rows = jnp.einsum(
            "tsc,td->scd", pick[:, :, part], tokens, preferred_element_type=jnp.float32
        ).astype(tokens.dtype)
        arrived = lax.all_to_all(send_rows, axes, split_axis=0, concat_axis=0, tiled=True)
        if k == 0:
            arrived, later_seed = lax.optimization_barrier((arrived, my_seed))
            weights = weights + (down_weight(later_seed),)
        results = expert_rows(arrived, weights)
        returned = lax.all_to_all(results, axes, split_axis=0, concat_axis=0, tiled=True)
        term = jnp.einsum(
            "tsc,scd->td", combine[:, :, part], returned,
            preferred_element_type=jnp.float32, precision=lax.Precision.HIGH,
        )
        out = term if out is None else out + term
    return out.astype(jnp.bfloat16)


def solution(mesh):
    in_specs = (
        P(("rep", "node", "local"), None),
        P(("rep", "node", "local"), None),
        P(("rep", "node", "local"), None),
        P(("rep", "node", "local"), None),
        P(("node", "local")),
    )
    out_specs = P(("rep", "node", "local"), None)
    return jax.shard_map(
        on_device, mesh=mesh, in_specs=in_specs, out_specs=out_specs, check_vma=False
    )
```

```python
import math

import numpy as np

import jax
import jax.numpy as jnp
from jax import lax
from jax.sharding import PartitionSpec as P

D = 7168
FF = 1024
TOP = 8
EXP_DEV = 4
CHUNKS = 2


route_scale = 2.5
salt_gate = 1013904223
salt_up = 1664525
salt_down = 22695477


def wrapped(value):
    return ((value + 2**31) % 2**32) - 2**31


def hashed_weight(expert_seed, salt_value, row_count, column_count, fan_in):
    row_index = lax.broadcasted_iota(jnp.int32, (row_count, 1), 0)
    column_index = lax.broadcasted_iota(jnp.int32, (1, column_count), 1)
    row_term = row_index * wrapped(column_count * 747796405) + (expert_seed * 1103515245 + salt_value)
    hashed = row_term + column_index * 747796405
    hashed = hashed ^ hashed >> 15
    hashed = hashed * 277803737
    hashed = hashed ^ hashed >> 13
    hashed = hashed * 668265263
    shifted_bits = ((hashed ^ hashed >> 16) & 0xFFFF00).astype(jnp.float32)
    scale = np.float32(math.sqrt(3.0 / fan_in) / 32768.0) / np.float32(256.0)
    return ((shifted_bits - np.float32(32767.5 * 256)) * scale).astype(jnp.bfloat16)


def expert_block(block_rows, expert_seed):
    weight_gate = hashed_weight(expert_seed, salt_gate, D, FF, D)
    weight_up = hashed_weight(expert_seed, salt_up, D, FF, D)
    weight_down = hashed_weight(expert_seed, salt_down, FF, D, FF)
    gate_part = jnp.dot(block_rows, weight_gate, preferred_element_type=jnp.float32)
    up_part = jnp.dot(block_rows, weight_up, preferred_element_type=jnp.float32)
    hidden = (jax.nn.silu(gate_part) * up_part).astype(jnp.bfloat16)
    return jnp.dot(hidden, weight_down, preferred_element_type=jnp.float32).astype(jnp.bfloat16)


def run_experts(expert_rows, local_seeds):

    def per_expert(running, scan_item):
        expert_seed, block_rows = scan_item
        return (running, expert_block(block_rows, expert_seed))

    unused, outputs = lax.scan(per_expert, jnp.zeros((), jnp.int32), (local_seeds, expert_rows))
    return outputs


def group_mask(expert_ids, node_groups, group_size):
    return jnp.any((expert_ids // group_size)[:, :, None] == node_groups[:, None, :], axis=2)


def gate_of(gate_levels, in_group):
    levels = gate_levels.astype(jnp.float32)
    return (
        route_scale * levels * in_group.astype(jnp.float32) / jnp.sum(levels, axis=1, keepdims=True)
    )


def rank_of(expert_ids, in_group, blocks, capacity, experts_total):
    expert_range = jnp.arange(experts_total, dtype=jnp.int32)
    hit_table = (
        (expert_ids[:, :, None] == expert_range[None, None, :]) & in_group[:, :, None]
    ).astype(jnp.int32)
    present = jnp.sum(hit_table, axis=1, dtype=jnp.int32)
    blocked = present.reshape(blocks, -1, experts_total)
    before = (jnp.cumsum(blocked, axis=1, dtype=jnp.int32) - blocked).reshape(-1, experts_total)
    slot_rank = jnp.sum(hit_table * before[:, None, :], axis=2, dtype=jnp.int32)
    kept_mask = in_group & (slot_rank < capacity)
    return (slot_rank, kept_mask)


def fill_slots(row_block, slot_index, slot_total):
    row_count = row_block.shape[0]
    token_index = lax.broadcasted_iota(jnp.int32, slot_index.shape, 0)
    slot_token = (
        jnp.full((slot_total,), row_count, jnp.int32)
        .at[slot_index.reshape(-1)]
        .set(token_index.reshape(-1), mode="drop")
    )
    padded = jnp.concatenate(
        [row_block, jnp.zeros((1, row_block.shape[1]), row_block.dtype)], axis=0
    )
    return padded[slot_token]


def combine_rows(returned, slot_index, gate_share):
    padded = jnp.concatenate([returned, jnp.zeros((1, returned.shape[1]), returned.dtype)], axis=0)
    picked = padded[slot_index]
    return jnp.einsum("tj,tjd->td", gate_share, picked.astype(jnp.float32))


def expert_weights(expert_seed):
    weight_gate = hashed_weight(expert_seed, salt_gate, D, FF, D)
    weight_up = hashed_weight(expert_seed, salt_up, D, FF, D)
    return lax.optimization_barrier((weight_gate, weight_up))


def down_weight(expert_seed):
    return lax.optimization_barrier(hashed_weight(expert_seed, salt_down, FF, D, FF))


def expert_rows(block_rows, weights):
    weight_gate, weight_up, weight_down = weights
    gate_part = jnp.einsum("sct,tf->scf", block_rows, weight_gate, preferred_element_type=jnp.float32)
    up_part = jnp.einsum("sct,tf->scf", block_rows, weight_up, preferred_element_type=jnp.float32)
    hidden = (jax.nn.silu(gate_part) * up_part).astype(jnp.bfloat16)
    return jnp.einsum("scf,ft->sct", hidden, weight_down, preferred_element_type=jnp.float32).astype(
        jnp.bfloat16
    )


def on_device(tokens, expert_ids, node_groups, gate_levels, expert_seeds):
    tok_count = tokens.shape[0]
    width = tokens.shape[1]
    axes = ("rep", "node", "local")
    rep_count = lax.axis_size("rep")
    plane_count = lax.axis_size(("node", "local"))
    local_count = lax.axis_size("local")
    seeds_here = expert_seeds.shape[0]
    assert seeds_here == rep_count
    experts_total = seeds_here * plane_count
    devices_all = experts_total
    capacity = max(2, tok_count * TOP // experts_total)
    group_size = seeds_here * local_count
    in_group = group_mask(expert_ids, node_groups, group_size)
    gate_share = gate_of(gate_levels, in_group)
    dest = (expert_ids % seeds_here) * plane_count + expert_ids // seeds_here
    device_range = jnp.arange(devices_all, dtype=jnp.int32)
    uses = (dest[:, :, None] == device_range[None, None, :]) & in_group[:, :, None]
    present = jnp.any(uses, axis=1)
    share = jnp.sum(jnp.where(uses, gate_share[:, :, None], 0.0), axis=1)
    counts = present.astype(jnp.int32)
    before = jnp.cumsum(counts, axis=0, dtype=jnp.int32) - counts
    slot_of = before[:, :, None] == jnp.arange(capacity, dtype=jnp.int32)[None, None, :]
    hit = present[:, :, None] & slot_of
    pick = hit.astype(tokens.dtype)
    combine = jnp.where(hit, share[:, :, None], 0.0)
    my_seed = expert_seeds[lax.axis_index("rep")]
    weights = expert_weights(my_seed)
    chunk = capacity // CHUNKS
    out = None
    for k in range(CHUNKS):
        part = slice(k * chunk, (k + 1) * chunk)
        send_rows = jnp.einsum(
            "tsc,td->scd", pick[:, :, part], tokens, preferred_element_type=jnp.float32
        ).astype(tokens.dtype)
        arrived = lax.all_to_all(send_rows, axes, split_axis=0, concat_axis=0, tiled=True)
        if k == 0:
            arrived, later_seed = lax.optimization_barrier((arrived, my_seed))
            weights = weights + (down_weight(later_seed),)
        results = expert_rows(arrived, weights)
        returned = lax.all_to_all(results, axes, split_axis=0, concat_axis=0, tiled=True)
        term = jnp.einsum(
            "tsc,scd->td", combine[:, :, part], returned,
            preferred_element_type=jnp.float32, precision=lax.Precision.HIGH,
        )
        out = term if out is None else out + term
    return out.astype(jnp.bfloat16)


def solution(mesh):
    in_specs = (
        P(("rep", "node", "local"), None),
        P(("rep", "node", "local"), None),
        P(("rep", "node", "local"), None),
        P(("rep", "node", "local"), None),
        P(("node", "local")),
    )
    out_specs = P(("rep", "node", "local"), None)
    return jax.shard_map(
        on_device, mesh=mesh, in_specs=in_specs, out_specs=out_specs, check_vma=False
    )
```

```python
import math

import numpy as np

import jax
import jax.numpy as jnp
from jax import lax
from jax.experimental import pallas as pl
from jax.sharding import PartitionSpec as P

D = 7168
FF = 1024
TOP = 8
EXP_DEV = 4
CHUNKS = 2


route_scale = 2.5
salt_gate = 1013904223
salt_up = 1664525
salt_down = 22695477


def wrapped(value):
    return ((value + 2**31) % 2**32) - 2**31


def hashed_weight(expert_seed, salt_value, row_count, column_count, fan_in):
    row_index = lax.broadcasted_iota(jnp.int32, (row_count, 1), 0)
    column_index = lax.broadcasted_iota(jnp.int32, (1, column_count), 1)
    row_term = row_index * wrapped(column_count * 747796405) + (expert_seed * 1103515245 + salt_value)
    hashed = row_term + column_index * 747796405
    hashed = hashed ^ hashed >> 15
    hashed = hashed * 277803737
    hashed = hashed ^ hashed >> 13
    hashed = hashed * 668265263
    shifted_bits = ((hashed ^ hashed >> 16) & 0xFFFF00).astype(jnp.float32)
    scale = np.float32(math.sqrt(3.0 / fan_in) / 32768.0) / np.float32(256.0)
    return ((shifted_bits - np.float32(32767.5 * 256)) * scale).astype(jnp.bfloat16)


def expert_block(block_rows, expert_seed):
    weight_gate = hashed_weight(expert_seed, salt_gate, D, FF, D)
    weight_up = hashed_weight(expert_seed, salt_up, D, FF, D)
    weight_down = hashed_weight(expert_seed, salt_down, FF, D, FF)
    gate_part = jnp.dot(block_rows, weight_gate, preferred_element_type=jnp.float32)
    up_part = jnp.dot(block_rows, weight_up, preferred_element_type=jnp.float32)
    hidden = (jax.nn.silu(gate_part) * up_part).astype(jnp.bfloat16)
    return jnp.dot(hidden, weight_down, preferred_element_type=jnp.float32).astype(jnp.bfloat16)


def run_experts(expert_rows, local_seeds):

    def per_expert(running, scan_item):
        expert_seed, block_rows = scan_item
        return (running, expert_block(block_rows, expert_seed))

    unused, outputs = lax.scan(per_expert, jnp.zeros((), jnp.int32), (local_seeds, expert_rows))
    return outputs


def group_mask(expert_ids, node_groups, group_size):
    return jnp.any((expert_ids // group_size)[:, :, None] == node_groups[:, None, :], axis=2)


def gate_of(gate_levels, in_group):
    levels = gate_levels.astype(jnp.float32)
    return (
        route_scale * levels * in_group.astype(jnp.float32) / jnp.sum(levels, axis=1, keepdims=True)
    )


def rank_of(expert_ids, in_group, blocks, capacity, experts_total):
    expert_range = jnp.arange(experts_total, dtype=jnp.int32)
    hit_table = (
        (expert_ids[:, :, None] == expert_range[None, None, :]) & in_group[:, :, None]
    ).astype(jnp.int32)
    present = jnp.sum(hit_table, axis=1, dtype=jnp.int32)
    blocked = present.reshape(blocks, -1, experts_total)
    before = (jnp.cumsum(blocked, axis=1, dtype=jnp.int32) - blocked).reshape(-1, experts_total)
    slot_rank = jnp.sum(hit_table * before[:, None, :], axis=2, dtype=jnp.int32)
    kept_mask = in_group & (slot_rank < capacity)
    return (slot_rank, kept_mask)


def fill_slots(row_block, slot_index, slot_total):
    row_count = row_block.shape[0]
    token_index = lax.broadcasted_iota(jnp.int32, slot_index.shape, 0)
    slot_token = (
        jnp.full((slot_total,), row_count, jnp.int32)
        .at[slot_index.reshape(-1)]
        .set(token_index.reshape(-1), mode="drop")
    )
    padded = jnp.concatenate(
        [row_block, jnp.zeros((1, row_block.shape[1]), row_block.dtype)], axis=0
    )
    return padded[slot_token]


def combine_rows(returned, slot_index, gate_share):
    padded = jnp.concatenate([returned, jnp.zeros((1, returned.shape[1]), returned.dtype)], axis=0)
    picked = padded[slot_index]
    return jnp.einsum("tj,tjd->td", gate_share, picked.astype(jnp.float32))


def _send_kernel(pick_lo_ref, pick_hi_ref, tokens_ref, out_ref):
    rows = tokens_ref[...]
    lo = jnp.dot(pick_lo_ref[...], rows, preferred_element_type=jnp.float32)
    hi = jnp.dot(pick_hi_ref[...], rows, preferred_element_type=jnp.float32)
    out_ref[...] = jnp.stack([lo.astype(out_ref.dtype), hi.astype(out_ref.dtype)], axis=1)


def send_rows_of(pick_part, tokens):
    devices_all = pick_part.shape[1]
    return pl.pallas_call(
        _send_kernel,
        out_shape=jax.ShapeDtypeStruct((devices_all, 2, tokens.shape[1]), tokens.dtype),
    )(pick_part[:, :, 0].T, pick_part[:, :, 1].T, tokens)


def expert_weights(expert_seed):
    weight_gate = hashed_weight(expert_seed, salt_gate, D, FF, D)
    weight_up = hashed_weight(expert_seed, salt_up, D, FF, D)
    return lax.optimization_barrier((weight_gate, weight_up))


def down_weight(expert_seed):
    return lax.optimization_barrier(hashed_weight(expert_seed, salt_down, FF, D, FF))


def expert_rows(block_rows, weights):
    weight_gate, weight_up, weight_down = weights
    gate_part = jnp.einsum("sct,tf->scf", block_rows, weight_gate, preferred_element_type=jnp.float32)
    up_part = jnp.einsum("sct,tf->scf", block_rows, weight_up, preferred_element_type=jnp.float32)
    hidden = (jax.nn.silu(gate_part) * up_part).astype(jnp.bfloat16)
    return jnp.einsum("scf,ft->sct", hidden, weight_down, preferred_element_type=jnp.float32).astype(
        jnp.bfloat16
    )


def on_device(tokens, expert_ids, node_groups, gate_levels, expert_seeds):
    tok_count = tokens.shape[0]
    width = tokens.shape[1]
    axes = ("rep", "node", "local")
    rep_count = lax.axis_size("rep")
    plane_count = lax.axis_size(("node", "local"))
    local_count = lax.axis_size("local")
    seeds_here = expert_seeds.shape[0]
    assert seeds_here == rep_count
    experts_total = seeds_here * plane_count
    devices_all = experts_total
    capacity = max(2, tok_count * TOP // experts_total)
    group_size = seeds_here * local_count
    in_group = group_mask(expert_ids, node_groups, group_size)
    gate_share = gate_of(gate_levels, in_group)
    dest = (expert_ids % seeds_here) * plane_count + expert_ids // seeds_here
    device_range = jnp.arange(devices_all, dtype=jnp.int32)
    uses = (dest[:, :, None] == device_range[None, None, :]) & in_group[:, :, None]
    present = jnp.any(uses, axis=1)
    share = jnp.sum(jnp.where(uses, gate_share[:, :, None], 0.0), axis=1)
    counts = present.astype(jnp.int32)
    before = jnp.cumsum(counts, axis=0, dtype=jnp.int32) - counts
    slot_of = before[:, :, None] == jnp.arange(capacity, dtype=jnp.int32)[None, None, :]
    hit = present[:, :, None] & slot_of
    pick = hit.astype(tokens.dtype)
    combine = jnp.where(hit, share[:, :, None], 0.0)
    my_seed = expert_seeds[lax.axis_index("rep")]
    weights = expert_weights(my_seed)
    chunk = capacity // CHUNKS
    out = None
    for k in range(CHUNKS):
        part = slice(k * chunk, (k + 1) * chunk)
        send_rows = send_rows_of(pick[:, :, part], tokens)
        arrived = lax.all_to_all(send_rows, axes, split_axis=0, concat_axis=0, tiled=True)
        if k == 0:
            arrived, later_seed = lax.optimization_barrier((arrived, my_seed))
            weights = weights + (down_weight(later_seed),)
        results = expert_rows(arrived, weights)
        returned = lax.all_to_all(results, axes, split_axis=0, concat_axis=0, tiled=True)
        term = jnp.einsum(
            "tsc,scd->td", combine[:, :, part], returned,
            preferred_element_type=jnp.float32, precision=lax.Precision.HIGH,
        )
        out = term if out is None else out + term
    return out.astype(jnp.bfloat16)


def solution(mesh):
    in_specs = (
        P(("rep", "node", "local"), None),
        P(("rep", "node", "local"), None),
        P(("rep", "node", "local"), None),
        P(("rep", "node", "local"), None),
        P(("node", "local")),
    )
    out_specs = P(("rep", "node", "local"), None)
    return jax.shard_map(
        on_device, mesh=mesh, in_specs=in_specs, out_specs=out_specs, check_vma=False
    )
```

```python
import math

import numpy as np

import jax
import jax.numpy as jnp
from jax import lax
from jax.sharding import PartitionSpec as P

D = 7168
FF = 1024
TOP = 8
EXP_DEV = 4
CHUNKS = 2


route_scale = 2.5
salt_gate = 1013904223
salt_up = 1664525
salt_down = 22695477


def wrapped(value):
    return ((value + 2**31) % 2**32) - 2**31


def hashed_weight(expert_seed, salt_value, row_count, column_count, fan_in):
    row_index = lax.broadcasted_iota(jnp.int32, (row_count, 1), 0)
    column_index = lax.broadcasted_iota(jnp.int32, (1, column_count), 1)
    row_term = row_index * wrapped(column_count * 747796405) + (expert_seed * 1103515245 + salt_value)
    hashed = row_term + column_index * 747796405
    hashed = hashed ^ hashed >> 15
    hashed = hashed * 277803737
    hashed = hashed ^ hashed >> 13
    hashed = hashed * 668265263
    shifted_bits = ((hashed ^ hashed >> 16) & 0xFFFF00).astype(jnp.float32)
    scale = np.float32(math.sqrt(3.0 / fan_in) / 32768.0) / np.float32(256.0)
    return ((shifted_bits - np.float32(32767.5 * 256)) * scale).astype(jnp.bfloat16)


def expert_block(block_rows, expert_seed):
    weight_gate = hashed_weight(expert_seed, salt_gate, D, FF, D)
    weight_up = hashed_weight(expert_seed, salt_up, D, FF, D)
    weight_down = hashed_weight(expert_seed, salt_down, FF, D, FF)
    gate_part = jnp.dot(block_rows, weight_gate, preferred_element_type=jnp.float32)
    up_part = jnp.dot(block_rows, weight_up, preferred_element_type=jnp.float32)
    hidden = (jax.nn.silu(gate_part) * up_part).astype(jnp.bfloat16)
    return jnp.dot(hidden, weight_down, preferred_element_type=jnp.float32).astype(jnp.bfloat16)


def run_experts(expert_rows, local_seeds):

    def per_expert(running, scan_item):
        expert_seed, block_rows = scan_item
        return (running, expert_block(block_rows, expert_seed))

    unused, outputs = lax.scan(per_expert, jnp.zeros((), jnp.int32), (local_seeds, expert_rows))
    return outputs


def group_mask(expert_ids, node_groups, group_size):
    return jnp.any((expert_ids // group_size)[:, :, None] == node_groups[:, None, :], axis=2)


def gate_of(gate_levels, in_group):
    levels = gate_levels.astype(jnp.float32)
    return (
        route_scale * levels * in_group.astype(jnp.float32) / jnp.sum(levels, axis=1, keepdims=True)
    )


def rank_of(expert_ids, in_group, blocks, capacity, experts_total):
    expert_range = jnp.arange(experts_total, dtype=jnp.int32)
    hit_table = (
        (expert_ids[:, :, None] == expert_range[None, None, :]) & in_group[:, :, None]
    ).astype(jnp.int32)
    present = jnp.sum(hit_table, axis=1, dtype=jnp.int32)
    blocked = present.reshape(blocks, -1, experts_total)
    before = (jnp.cumsum(blocked, axis=1, dtype=jnp.int32) - blocked).reshape(-1, experts_total)
    slot_rank = jnp.sum(hit_table * before[:, None, :], axis=2, dtype=jnp.int32)
    kept_mask = in_group & (slot_rank < capacity)
    return (slot_rank, kept_mask)


def fill_slots(row_block, slot_index, slot_total):
    row_count = row_block.shape[0]
    token_index = lax.broadcasted_iota(jnp.int32, slot_index.shape, 0)
    slot_token = (
        jnp.full((slot_total,), row_count, jnp.int32)
        .at[slot_index.reshape(-1)]
        .set(token_index.reshape(-1), mode="drop")
    )
    padded = jnp.concatenate(
        [row_block, jnp.zeros((1, row_block.shape[1]), row_block.dtype)], axis=0
    )
    return padded[slot_token]


def combine_rows(returned, slot_index, gate_share):
    padded = jnp.concatenate([returned, jnp.zeros((1, returned.shape[1]), returned.dtype)], axis=0)
    picked = padded[slot_index]
    return jnp.einsum("tj,tjd->td", gate_share, picked.astype(jnp.float32))


def expert_weights(expert_seed):
    weight_gate = hashed_weight(expert_seed, salt_gate, D, FF, D)
    weight_up = hashed_weight(expert_seed, salt_up, D, FF, D)
    return lax.optimization_barrier((weight_gate, weight_up))


def down_weight(expert_seed):
    return lax.optimization_barrier(hashed_weight(expert_seed, salt_down, FF, D, FF))


def expert_rows(block_rows, weights):
    weight_gate, weight_up, weight_down = weights
    gate_part = jnp.einsum("sct,tf->scf", block_rows, weight_gate, preferred_element_type=jnp.float32)
    up_part = jnp.einsum("sct,tf->scf", block_rows, weight_up, preferred_element_type=jnp.float32)
    hidden = (jax.nn.silu(gate_part) * up_part).astype(jnp.bfloat16)
    return jnp.einsum("scf,ft->sct", hidden, weight_down, preferred_element_type=jnp.float32).astype(
        jnp.bfloat16
    )


def on_device(tokens, expert_ids, node_groups, gate_levels, expert_seeds):
    tok_count = tokens.shape[0]
    width = tokens.shape[1]
    axes = ("rep", "node", "local")
    rep_count = lax.axis_size("rep")
    plane_count = lax.axis_size(("node", "local"))
    local_count = lax.axis_size("local")
    seeds_here = expert_seeds.shape[0]
    assert seeds_here == rep_count
    experts_total = seeds_here * plane_count
    devices_all = experts_total
    capacity = max(2, tok_count * TOP // experts_total)
    group_size = seeds_here * local_count
    in_group = group_mask(expert_ids, node_groups, group_size)
    gate_share = gate_of(gate_levels, in_group)
    dest = (expert_ids % seeds_here) * plane_count + expert_ids // seeds_here
    device_range = jnp.arange(devices_all, dtype=jnp.int32)
    uses = (dest[:, :, None] == device_range[None, None, :]) & in_group[:, :, None]
    present = jnp.any(uses, axis=1)
    share = jnp.sum(jnp.where(uses, gate_share[:, :, None], 0.0), axis=1)
    counts = present.astype(jnp.int32)
    before = jnp.cumsum(counts, axis=0, dtype=jnp.int32) - counts
    slot_of = before[:, :, None] == jnp.arange(capacity, dtype=jnp.int32)[None, None, :]
    hit = present[:, :, None] & slot_of
    pick = hit.astype(tokens.dtype)
    combine = jnp.where(hit, share[:, :, None], 0.0)
    my_seed = expert_seeds[lax.axis_index("rep")]
    weights = expert_weights(my_seed)
    chunk = capacity // CHUNKS
    out = None
    for k in range(CHUNKS):
        part = slice(k * chunk, (k + 1) * chunk)
        send_rows = jnp.einsum(
            "tsc,td->scd", pick[:, :, part], tokens, preferred_element_type=jnp.float32
        ).astype(tokens.dtype)
        arrived = lax.all_to_all(send_rows, axes, split_axis=0, concat_axis=0, tiled=True)
        if k == 0:
            arrived, later_seed = lax.optimization_barrier((arrived, my_seed))
            weights = weights + (down_weight(later_seed),)
        results = expert_rows(arrived, weights)
        returned = lax.all_to_all(results, axes, split_axis=0, concat_axis=0, tiled=True)
        term = jnp.einsum(
            "tsc,scd->td", combine[:, :, part], returned,
            preferred_element_type=jnp.float32,
        )
        out = term if out is None else out + term
    return out.astype(jnp.bfloat16)


def solution(mesh):
    in_specs = (
        P(("rep", "node", "local"), None),
        P(("rep", "node", "local"), None),
        P(("rep", "node", "local"), None),
        P(("rep", "node", "local"), None),
        P(("node", "local")),
    )
    out_specs = P(("rep", "node", "local"), None)
    return jax.shard_map(
        on_device, mesh=mesh, in_specs=in_specs, out_specs=out_specs, check_vma=False
    )
```

```python
import math

import numpy as np

import jax
import jax.numpy as jnp
from jax import lax
from jax.sharding import PartitionSpec as P

D = 7168
FF = 1024
TOP = 8
EXP_DEV = 4
CHUNKS = 2


route_scale = 2.5
salt_gate = 1013904223
salt_up = 1664525
salt_down = 22695477


def wrapped(value):
    return ((value + 2**31) % 2**32) - 2**31


def hashed_weight(expert_seed, salt_value, row_count, column_count, fan_in):
    row_index = lax.broadcasted_iota(jnp.int32, (row_count, 1), 0)
    column_index = lax.broadcasted_iota(jnp.int32, (1, column_count), 1)
    row_term = row_index * wrapped(column_count * 747796405) + (expert_seed * 1103515245 + salt_value)
    hashed = row_term + column_index * 747796405
    hashed = hashed ^ hashed >> 15
    hashed = hashed * 277803737
    hashed = hashed ^ hashed >> 13
    hashed = hashed * 668265263
    shifted_bits = ((hashed ^ hashed >> 16) & 0xFFFF00).astype(jnp.float32)
    scale = np.float32(math.sqrt(3.0 / fan_in) / 32768.0) / np.float32(256.0)
    return ((shifted_bits - np.float32(32767.5 * 256)) * scale).astype(jnp.bfloat16)


def expert_block(block_rows, expert_seed):
    weight_gate = hashed_weight(expert_seed, salt_gate, D, FF, D)
    weight_up = hashed_weight(expert_seed, salt_up, D, FF, D)
    weight_down = hashed_weight(expert_seed, salt_down, FF, D, FF)
    gate_part = jnp.dot(block_rows, weight_gate, preferred_element_type=jnp.float32)
    up_part = jnp.dot(block_rows, weight_up, preferred_element_type=jnp.float32)
    hidden = (jax.nn.silu(gate_part) * up_part).astype(jnp.bfloat16)
    return jnp.dot(hidden, weight_down, preferred_element_type=jnp.float32).astype(jnp.bfloat16)


def run_experts(expert_rows, local_seeds):

    def per_expert(running, scan_item):
        expert_seed, block_rows = scan_item
        return (running, expert_block(block_rows, expert_seed))

    unused, outputs = lax.scan(per_expert, jnp.zeros((), jnp.int32), (local_seeds, expert_rows))
    return outputs


def group_mask(expert_ids, node_groups, group_size):
    return jnp.any((expert_ids // group_size)[:, :, None] == node_groups[:, None, :], axis=2)


def gate_of(gate_levels, in_group):
    levels = gate_levels.astype(jnp.float32)
    return (
        route_scale * levels * in_group.astype(jnp.float32) / jnp.sum(levels, axis=1, keepdims=True)
    )


def rank_of(expert_ids, in_group, blocks, capacity, experts_total):
    expert_range = jnp.arange(experts_total, dtype=jnp.int32)
    hit_table = (
        (expert_ids[:, :, None] == expert_range[None, None, :]) & in_group[:, :, None]
    ).astype(jnp.int32)
    present = jnp.sum(hit_table, axis=1, dtype=jnp.int32)
    blocked = present.reshape(blocks, -1, experts_total)
    before = (jnp.cumsum(blocked, axis=1, dtype=jnp.int32) - blocked).reshape(-1, experts_total)
    slot_rank = jnp.sum(hit_table * before[:, None, :], axis=2, dtype=jnp.int32)
    kept_mask = in_group & (slot_rank < capacity)
    return (slot_rank, kept_mask)


def fill_slots(row_block, slot_index, slot_total):
    row_count = row_block.shape[0]
    token_index = lax.broadcasted_iota(jnp.int32, slot_index.shape, 0)
    slot_token = (
        jnp.full((slot_total,), row_count, jnp.int32)
        .at[slot_index.reshape(-1)]
        .set(token_index.reshape(-1), mode="drop")
    )
    padded = jnp.concatenate(
        [row_block, jnp.zeros((1, row_block.shape[1]), row_block.dtype)], axis=0
    )
    return padded[slot_token]


def combine_rows(returned, slot_index, gate_share):
    padded = jnp.concatenate([returned, jnp.zeros((1, returned.shape[1]), returned.dtype)], axis=0)
    picked = padded[slot_index]
    return jnp.einsum("tj,tjd->td", gate_share, picked.astype(jnp.float32))


def expert_weights(expert_seed):
    weight_gate = hashed_weight(expert_seed, salt_gate, D, FF, D)
    weight_up = hashed_weight(expert_seed, salt_up, D, FF, D)
    return lax.optimization_barrier((weight_gate, weight_up))


def down_weight(expert_seed):
    return lax.optimization_barrier(hashed_weight(expert_seed, salt_down, FF, D, FF))


def expert_rows(block_rows, weights):
    weight_gate, weight_up, weight_down = weights
    gate_part = jnp.einsum("sct,tf->scf", block_rows, weight_gate, preferred_element_type=jnp.float32)
    up_part = jnp.einsum("sct,tf->scf", block_rows, weight_up, preferred_element_type=jnp.float32)
    hidden = (jax.nn.silu(gate_part) * up_part).astype(jnp.bfloat16)
    return jnp.einsum("scf,ft->sct", hidden, weight_down, preferred_element_type=jnp.float32).astype(
        jnp.bfloat16
    )


def on_device(tokens, expert_ids, node_groups, gate_levels, expert_seeds):
    tok_count = tokens.shape[0]
    width = tokens.shape[1]
    axes = ("rep", "node", "local")
    rep_count = lax.axis_size("rep")
    plane_count = lax.axis_size(("node", "local"))
    local_count = lax.axis_size("local")
    seeds_here = expert_seeds.shape[0]
    assert seeds_here == rep_count
    experts_total = seeds_here * plane_count
    devices_all = experts_total
    capacity = max(2, tok_count * TOP // experts_total)
    group_size = seeds_here * local_count
    seed_bits = seeds_here.bit_length() - 1
    group_bits = group_size.bit_length() - 1
    assert seeds_here == 1 << seed_bits and group_size == 1 << group_bits
    expert_group = lax.shift_right_logical(expert_ids, group_bits)
    in_group = jnp.any(expert_group[:, :, None] == node_groups[:, None, :], axis=2)
    gate_share = gate_of(gate_levels, in_group)
    dest = (expert_ids & (seeds_here - 1)) * plane_count + lax.shift_right_logical(expert_ids, seed_bits)
    device_range = jnp.arange(devices_all, dtype=jnp.int32)
    uses = (dest[:, :, None] == device_range[None, None, :]) & in_group[:, :, None]
    present = jnp.any(uses, axis=1)
    share = jnp.sum(jnp.where(uses, gate_share[:, :, None], 0.0), axis=1)
    counts = present.astype(jnp.int32)
    before = jnp.cumsum(counts, axis=0, dtype=jnp.int32) - counts
    slot_of = before[:, :, None] == jnp.arange(capacity, dtype=jnp.int32)[None, None, :]
    hit = present[:, :, None] & slot_of
    pick = hit.astype(tokens.dtype)
    combine = jnp.where(hit, share[:, :, None], 0.0)
    my_seed = expert_seeds[lax.axis_index("rep")]
    weights = expert_weights(my_seed)
    chunk = capacity // CHUNKS
    out = None
    for k in range(CHUNKS):
        part = slice(k * chunk, (k + 1) * chunk)
        send_rows = jnp.einsum(
            "tsc,td->scd", pick[:, :, part], tokens, preferred_element_type=jnp.float32
        ).astype(tokens.dtype)
        arrived = lax.all_to_all(send_rows, axes, split_axis=0, concat_axis=0, tiled=True)
        if k == 0:
            arrived, later_seed = lax.optimization_barrier((arrived, my_seed))
            weights = weights + (down_weight(later_seed),)
        results = expert_rows(arrived, weights)
        returned = lax.all_to_all(results, axes, split_axis=0, concat_axis=0, tiled=True)
        term = jnp.einsum(
            "tsc,scd->td", combine[:, :, part], returned,
            preferred_element_type=jnp.float32,
        )
        out = term if out is None else out + term
    return out.astype(jnp.bfloat16)


def solution(mesh):
    in_specs = (
        P(("rep", "node", "local"), None),
        P(("rep", "node", "local"), None),
        P(("rep", "node", "local"), None),
        P(("rep", "node", "local"), None),
        P(("node", "local")),
    )
    out_specs = P(("rep", "node", "local"), None)
    return jax.shard_map(
        on_device, mesh=mesh, in_specs=in_specs, out_specs=out_specs, check_vma=False
    )
```
